256 devices in a mesh: row: 8 (over x_hi, y), feat: 32 (over x_lo, z, core).
Axes of the slice: x: 4 (x_hi: 2, x_lo: 2; x = x_hi * 2 + x_lo), y: 4, z: 8, core: 2. Of those that a mesh axis runs over, the one named last changes fastest.
Arguments:
- node_features: bfloat16 [1024, 65536], P('feat', 'row'), may hold values from -6 to 6
- adjacency: bfloat16 [2048, 128, 128], P('row'), may hold values from -0.5 to 0.5
- tile_row: int32 [2048], P('row'), may hold values from 0 to 63
- tile_col: int32 [2048], P('row'), may hold values from 0 to 63
- tile_count: int32 [8, 8], P('row'), may hold values from 1 to 32, as said below
- weight: bfloat16 [1024, 1024], P('feat'), may hold values from -0.1875 to 0.1875
- out_bias: float32 [1024], replicated, may hold values from -3 to 3
Outputs:
- activated: bfloat16 [1024, 65536], P('feat', 'row')
The draws below stay inside these ranges and needn't reach their ends.
Inputs may be any that keep to these rules, and one draw needn't show every extreme that they name: tile_count[r, s] is at least 1; the entry with s equal to r is 32.
All inputs are finite; a program needn't handle non-finite values.
Results may differ from the reference program's by a relative error of at most 0.0095.
Values may be sent and summed in bfloat16 or wider, within the bound.
No kernel may reach another device: no remote copies, remote signals or barrier semaphores. Data moves between devices by JAX's collectives and lax.ppermute only.
A program may use at most 128 MiB of HBM per device.

```python
import jax
import jax.numpy as jnp

F = 1024
TILE = 128
ROWS_DEV = 8192
SLOTS = 32
NODES = 65536
N_ROW = 8


def draw_tile_count(key, part):
    first_key, second_key = jax.random.split(key)
    first_draw = jax.random.randint(first_key, (N_ROW, N_ROW), 1, SLOTS + 1)
    second_draw = jax.random.randint(second_key, (N_ROW, N_ROW), 1, SLOTS + 1)
    lesser = jnp.minimum(first_draw, second_draw)
    index_list = jnp.arange(N_ROW)
    diagonal = index_list[:, None] == index_list[None, :]
    return jnp.where(diagonal, SLOTS, lesser).astype(jnp.int32)


def plant(values, own_key, least, largest):
    spot = [jax.random.randint(jax.random.fold_in(own_key, axis), (), 0, length) for axis, length in enumerate(values.shape)]
    longest = values.shape.index(max(values.shape))
    neighbour = spot[:longest] + [(spot[longest] + 1) % values.shape[longest]] + spot[longest + 1:]
    return values.at[tuple(spot)].set(least).at[tuple(neighbour)].set(largest)


def levels(own_key, shape, pieces, smallest, high):
    def one(axis_at, shards_of):
        steps = jax.random.uniform(jax.random.fold_in(jax.random.fold_in(own_key, 6), axis_at), (shards_of,), jnp.float32, smallest / len(pieces), high / len(pieces))
        return jnp.repeat(jnp.exp(steps), shape[axis_at] // shards_of).reshape((-1,) + (1,) * (len(shape) - axis_at - 1))

    level = one(*pieces[0])
    for cut in pieces[1:]:
        level = level * one(*cut)
    return level


def normal_values(stream_key, dims, width, bound, shards=(), held_as=jnp.bfloat16):
    gain = levels(stream_key, dims, shards, -0.22, 0.18) if shards else 1.0
    array = jax.random.normal(stream_key, dims, jnp.float32) * width * gain
    return jnp.minimum(jnp.maximum(array, -bound), bound).astype(held_as)


def setup_inputs(seed: int = 0) -> dict:
    key_list = jax.random.split(jax.random.key(seed), 8)
    return {
        "node_features": normal_values(key_list[0], (F, NODES), 1.0, 6.0, ((0, 32), (1, 8))),
        "adjacency": normal_values(key_list[1], (N_ROW * N_ROW * SLOTS, TILE, TILE), TILE ** -0.5, 0.5, ((0, 8),)),
        "tile_row": plant(jax.random.randint(key_list[2], (N_ROW * N_ROW * SLOTS,), 0, ROWS_DEV // TILE), jax.random.fold_in(key_list[2], 1), 0, (ROWS_DEV // TILE) - 1).astype(jnp.int32),
        "tile_col": plant(jax.random.randint(key_list[3], (N_ROW * N_ROW * SLOTS,), 0, ROWS_DEV // TILE), jax.random.fold_in(key_list[3], 1), 0, (ROWS_DEV // TILE) - 1).astype(jnp.int32),
        "tile_count": draw_tile_count(jax.random.fold_in(key_list[7], 71), 0),
        "weight": normal_values(key_list[5], (F, F), F ** -0.5, 0.1875, ((0, 32),)),
        "out_bias": normal_values(key_list[6], (F,), 0.5, 3.0, (), jnp.float32),
    }


def source_term(held_block, tiles_part, rows_part, cols_part, live_count, row_blocks):
    feat_width = held_block.shape[0]
    blocks = held_block.reshape(feat_width, row_blocks, TILE)
    picked = jnp.take(blocks, cols_part, axis=1).astype(jnp.float32)
    product = jnp.einsum("fsj,sji->fsi", picked, tiles_part.astype(jnp.float32))
    slot_ids = jnp.arange(rows_part.shape[0]).astype(jnp.int32)
    live_mask = slot_ids < live_count
    block_ids = jnp.arange(row_blocks).astype(jnp.int32)
    onehot = ((rows_part[:, None] == block_ids[None, :]) & live_mask[:, None]).astype(jnp.float32)
    return jnp.einsum("fsi,sr->fri", product, onehot)


def reference(node_features, adjacency, tile_row, tile_col, tile_count, weight, out_bias):
    row_blocks = ROWS_DEV // TILE
    columns_out = []
    for row_dev in range(N_ROW):
        running = jnp.zeros((F, row_blocks, TILE), jnp.float32)
        for src_dev in range(N_ROW):
            first_slot = (row_dev * N_ROW + src_dev) * SLOTS
            running = running + source_term(
                node_features[:, src_dev * ROWS_DEV:(src_dev + 1) * ROWS_DEV],
                adjacency[first_slot:first_slot + SLOTS],
                tile_row[first_slot:first_slot + SLOTS],
                tile_col[first_slot:first_slot + SLOTS],
                tile_count[row_dev, src_dev],
                row_blocks)
        aggregated = running.reshape(F, ROWS_DEV).astype(jnp.bfloat16)
        pre_act = jnp.dot(weight, aggregated, preferred_element_type=jnp.float32) + out_bias[:, None]
        columns_out.append(jax.nn.relu(pre_act).astype(jnp.bfloat16))
    return jnp.concatenate(columns_out, axis=1)
```

```python
import jax
import jax.numpy as jnp
from jax import lax
from jax.sharding import PartitionSpec as P


def from_behind(value, axis, steps):
    count = lax.axis_size(axis)
    pairs = [(source, (source + steps) % count) for source in range(count)]
    return lax.ppermute(value, axis, pairs)


def on_device(node_features, adjacency, tile_row, tile_col, tile_count, weight, out_bias):
    feat_width = node_features.shape[0]
    rows_here = node_features.shape[1]
    tile_size = adjacency.shape[1]
    row_blocks = rows_here // tile_size
    slot_total = tile_row.shape[0] // lax.axis_size("row")
    cycle_len = lax.axis_size("row")
    feat_count = lax.axis_size("feat")
    own_row = lax.axis_index("row")
    counts_here = tile_count[0]
    block_ids = jnp.arange(row_blocks)
    slot_ids = jnp.arange(slot_total)

    w_full = lax.all_gather(weight, "feat", axis=0, tiled=True)

    def add_source(running, held_block, source):
        first_slot = source * slot_total
        tiles_part = lax.dynamic_slice_in_dim(adjacency, first_slot, slot_total, 0)
        rows_part = lax.dynamic_slice_in_dim(tile_row, first_slot, slot_total, 0)
        cols_part = lax.dynamic_slice_in_dim(tile_col, first_slot, slot_total, 0)
        live_count = lax.dynamic_index_in_dim(counts_here, source, 0, keepdims=False)
        blocks = held_block.reshape(feat_width, row_blocks, tile_size)
        picked = jnp.take(blocks, cols_part, axis=1)
        product = jnp.einsum("fsj,sji->fsi", picked, tiles_part, preferred_element_type=jnp.float32)
        live_mask = slot_ids < live_count
        onehot = ((rows_part[:, None] == block_ids[None, :]) & live_mask[:, None]).astype(
            jnp.float32
        )
        return running + jnp.einsum("fsi,sr->fri", product, onehot)

    held = [from_behind(node_features, "row", k) for k in range(1, cycle_len)]
    running = jnp.zeros((feat_width, row_blocks, tile_size), jnp.float32)
    running = add_source(running, node_features, own_row)
    for step_num in range(1, cycle_len):
        running = add_source(running, held[step_num - 1], (own_row - step_num) % cycle_len)
    aggregated = running.reshape(feat_width, rows_here).astype(jnp.bfloat16)
    agg_t = lax.all_to_all(aggregated, "feat", 1, 0, tiled=True)
    pre_act = jnp.dot(w_full, agg_t, preferred_element_type=jnp.float32)
    act_t = jax.nn.relu(pre_act + out_bias[:, None]).astype(jnp.bfloat16)
    activated = lax.all_to_all(act_t, "feat", 0, 1, tiled=True)
    return activated


def solution(mesh):
    in_specs = (
        P("feat", "row"),
        P("row", None, None),
        P("row"),
        P("row"),
        P("row", None),
        P("feat", None),
        P(),
    )
    out_specs = P("feat", "row")
    return jax.shard_map(
        on_device, mesh=mesh, in_specs=in_specs, out_specs=out_specs, check_vma=False
    )
```

```python
import jax
import jax.numpy as jnp
from jax import lax
from jax.sharding import PartitionSpec as P


def from_behind(value, axis, steps):
    count = lax.axis_size(axis)
    pairs = [(source, (source + steps) % count) for source in range(count)]
    return lax.ppermute(value, axis, pairs)


def on_device(node_features, adjacency, tile_row, tile_col, tile_count, weight, out_bias):
    feat_width = node_features.shape[0]
    rows_here = node_features.shape[1]
    tile_size = adjacency.shape[1]
    row_blocks = rows_here // tile_size
    cycle_len = lax.axis_size("row")
    slot_total = tile_row.shape[0] // cycle_len
    own_row = lax.axis_index("row")
    counts_here = tile_count[0]
    block_ids = jnp.arange(row_blocks)
    slot_ids = jnp.arange(slot_total)

    w_full = lax.all_gather(weight, "feat", axis=0, tiled=True)
    cols_out = lax.all_to_all(tile_col.reshape(cycle_len, slot_total), "row", 0, 0, tiled=True)
    blocks = node_features.reshape(feat_width, row_blocks, tile_size)

    def add_source(running, picked, source):
        first_slot = source * slot_total
        tiles_part = lax.dynamic_slice_in_dim(adjacency, first_slot, slot_total, 0)
        rows_part = lax.dynamic_slice_in_dim(tile_row, first_slot, slot_total, 0)
        live_count = lax.dynamic_index_in_dim(counts_here, source, 0, keepdims=False)
        product = jnp.einsum("fsj,sji->fsi", picked, tiles_part, preferred_element_type=jnp.float32)
        live_mask = slot_ids < live_count
        onehot = ((rows_part[:, None] == block_ids[None, :]) & live_mask[:, None]).astype(
            jnp.float32
        )
        return running + jnp.einsum("fsi,sr->fri", product, onehot)

    held = []
    for k in range(1, cycle_len):
        dest = (own_row + k) % cycle_len
        cols_k = lax.dynamic_index_in_dim(cols_out, dest, 0, keepdims=False)
        held.append(from_behind(jnp.take(blocks, cols_k, axis=1), "row", k))
    own_cols = lax.dynamic_slice_in_dim(tile_col, own_row * slot_total, slot_total, 0)
    running = jnp.zeros((feat_width, row_blocks, tile_size), jnp.float32)
    running = add_source(running, jnp.take(blocks, own_cols, axis=1), own_row)
    for step_num in range(1, cycle_len):
        running = add_source(running, held[step_num - 1], (own_row - step_num) % cycle_len)
    aggregated = running.reshape(feat_width, rows_here).astype(jnp.bfloat16)
    agg_t = lax.all_to_all(aggregated, "feat", 1, 0, tiled=True)
    pre_act = jnp.dot(w_full, agg_t, preferred_element_type=jnp.float32)
    act_t = jax.nn.relu(pre_act + out_bias[:, None]).astype(jnp.bfloat16)
    activated = lax.all_to_all(act_t, "feat", 0, 1, tiled=True)
    return activated


def solution(mesh):
    in_specs = (
        P("feat", "row"),
        P("row", None, None),
        P("row"),
        P("row"),
        P("row", None),
        P("feat", None),
        P(),
    )
    out_specs = P("feat", "row")
    return jax.shard_map(
        on_device, mesh=mesh, in_specs=in_specs, out_specs=out_specs, check_vma=False
    )
```

```python
import jax
import jax.numpy as jnp
from jax import lax
from jax.sharding import PartitionSpec as P


def from_behind(value, axis, steps):
    count = lax.axis_size(axis)
    pairs = [(source, (source + steps) % count) for source in range(count)]
    return lax.ppermute(value, axis, pairs)


def on_device(node_features, adjacency, tile_row, tile_col, tile_count, weight, out_bias):
    feat_width = node_features.shape[0]
    rows_here = node_features.shape[1]
    tile_size = adjacency.shape[1]
    row_blocks = rows_here // tile_size
    cycle_len = lax.axis_size("row")
    slot_total = tile_row.shape[0] // cycle_len
    own_row = lax.axis_index("row")
    counts_here = tile_count[0]

    w_full = lax.all_gather(weight, "feat", axis=0, tiled=True)
    cols_out = lax.all_to_all(tile_col.reshape(cycle_len, slot_total), "row", 0, 0, tiled=True)
    blocks_t = node_features.reshape(feat_width, row_blocks, tile_size).transpose(1, 0, 2)

    tile_ids = jnp.arange(cycle_len * slot_total)
    live_all = (tile_ids % slot_total) < counts_here[tile_ids // slot_total]
    onehot_all = (
        (tile_row[:, None] == jnp.arange(row_blocks)[None, :]) & live_all[:, None]
    ).astype(jnp.float32).reshape(cycle_len, slot_total, row_blocks)

    def add_source(running, picked, source):
        tiles_part = lax.dynamic_slice_in_dim(adjacency, source * slot_total, slot_total, 0)
        onehot = lax.dynamic_index_in_dim(onehot_all, source, 0, keepdims=False)
        product = jnp.einsum("sfj,sji->fsi", picked, tiles_part, preferred_element_type=jnp.float32)
        return running + jnp.einsum("fsi,sr->fri", product, onehot)

    dests = (own_row + jnp.arange(1, cycle_len)) % cycle_len
    send_cols = jnp.take(cols_out, dests, axis=0).reshape(-1)
    picked_all = jnp.take(blocks_t, send_cols, axis=0).reshape(
        cycle_len - 1, slot_total, feat_width, tile_size
    )
    held = [from_behind(picked_all[k - 1], "row", k) for k in range(1, cycle_len)]
    own_cols = lax.dynamic_slice_in_dim(tile_col, own_row * slot_total, slot_total, 0)
    running = jnp.zeros((feat_width, row_blocks, tile_size), jnp.float32)
    running = add_source(running, jnp.take(blocks_t, own_cols, axis=0), own_row)
    for step_num in range(1, cycle_len):
        running = add_source(running, held[step_num - 1], (own_row - step_num) % cycle_len)
    aggregated = running.reshape(feat_width, rows_here).astype(jnp.bfloat16)
    agg_t = lax.all_to_all(aggregated, "feat", 1, 0, tiled=True)
    pre_act = jnp.dot(w_full, agg_t, preferred_element_type=jnp.float32)
    act_t = jax.nn.relu(pre_act + out_bias[:, None]).astype(jnp.bfloat16)
    activated = lax.all_to_all(act_t, "feat", 0, 1, tiled=True)
    return activated


def solution(mesh):
    in_specs = (
        P("feat", "row"),
        P("row", None, None),
        P("row"),
        P("row"),
        P("row", None),
        P("feat", None),
        P(),
    )
    out_specs = P("feat", "row")
    return jax.shard_map(
        on_device, mesh=mesh, in_specs=in_specs, out_specs=out_specs, check_vma=False
    )
```

```python
import jax
import jax.numpy as jnp
from jax import lax
from jax.sharding import PartitionSpec as P


def from_behind(value, axis, steps):
    count = lax.axis_size(axis)
    pairs = [(source, (source + steps) % count) for source in range(count)]
    return lax.ppermute(value, axis, pairs)


def feat_permute(value, target):
    count = lax.axis_size("feat")
    return lax.ppermute(value, "feat", [(f, target(f)) for f in range(count)])


def gather_weight(weight):
    z_len = lax.axis_size("feat") // 4
    me = lax.axis_index("feat")
    own_core = me % 2
    own_z = (me // 2) % z_len
    own_xlo = me // (2 * z_len)
    xlo_stride = 2 * z_len
    partner = feat_permute(weight, lambda f: f ^ xlo_stride)
    pair = jnp.where(own_xlo == 0, jnp.stack([weight, partner]), jnp.stack([partner, weight]))
    got = [pair] + [
        feat_permute(pair, lambda f, k=k: (f // xlo_stride) * xlo_stride + ((f // 2 + k) % z_len) * 2 + f % 2)
        for k in range(1, z_len)
    ]
    order = (own_z - jnp.arange(z_len)) % z_len
    by_z = jnp.take(jnp.stack(got), order, axis=0)
    other = feat_permute(by_z, lambda f: f ^ 1)
    by_core = jnp.where(own_core == 0, jnp.stack([by_z, other]), jnp.stack([other, by_z]))
    return by_core.transpose(2, 1, 0, 3, 4).reshape(-1, weight.shape[1])


def on_device(node_features, adjacency, tile_row, tile_col, tile_count, weight, out_bias):
    feat_width = node_features.shape[0]
    rows_here = node_features.shape[1]
    tile_size = adjacency.shape[1]
    row_blocks = rows_here // tile_size
    cycle_len = lax.axis_size("row")
    slot_total = tile_row.shape[0] // cycle_len
    own_row = lax.axis_index("row")
    counts_here = tile_count[0]

    w_full = gather_weight(weight)
    cols_out = lax.all_to_all(tile_col.reshape(cycle_len, slot_total), "row", 0, 0, tiled=True)
    blocks_t = node_features.reshape(feat_width, row_blocks, tile_size).transpose(1, 0, 2)

    tile_ids = jnp.arange(cycle_len * slot_total)
    live_all = (tile_ids % slot_total) < counts_here[tile_ids // slot_total]
    onehot_all = (
        (tile_row[:, None] == jnp.arange(row_blocks)[None, :]) & live_all[:, None]
    ).astype(jnp.float32).reshape(cycle_len, slot_total, row_blocks)

    def add_source(running, picked, source):
        tiles_part = lax.dynamic_slice_in_dim(adjacency, source * slot_total, slot_total, 0)
        onehot = lax.dynamic_index_in_dim(onehot_all, source, 0, keepdims=False)
        product = jnp.einsum("sfj,sji->fsi", picked, tiles_part, preferred_element_type=jnp.float32)
        return running + jnp.einsum("fsi,sr->fri", product, onehot)

    dests = (own_row + jnp.arange(1, cycle_len)) % cycle_len
    send_cols = jnp.take(cols_out, dests, axis=0).reshape(-1)
    picked_all = jnp.take(blocks_t, send_cols, axis=0).reshape(
        cycle_len - 1, slot_total, feat_width, tile_size
    )
    held = [from_behind(picked_all[k - 1], "row", k) for k in range(1, cycle_len)]
    own_cols = lax.dynamic_slice_in_dim(tile_col, own_row * slot_total, slot_total, 0)
    running = jnp.zeros((feat_width, row_blocks, tile_size), jnp.float32)
    running = add_source(running, jnp.take(blocks_t, own_cols, axis=0), own_row)
    for step_num in range(1, cycle_len):
        running = add_source(running, held[step_num - 1], (own_row - step_num) % cycle_len)
    aggregated = running.reshape(feat_width, rows_here).astype(jnp.bfloat16)
    agg_t = lax.all_to_all(aggregated, "feat", 1, 0, tiled=True)
    pre_act = jnp.dot(w_full, agg_t, preferred_element_type=jnp.float32)
    act_t = jax.nn.relu(pre_act + out_bias[:, None]).astype(jnp.bfloat16)
    activated = lax.all_to_all(act_t, "feat", 0, 1, tiled=True)
    return activated


def solution(mesh):
    in_specs = (
        P("feat", "row"),
        P("row", None, None),
        P("row"),
        P("row"),
        P("row", None),
        P("feat", None),
        P(),
    )
    out_specs = P("feat", "row")
    return jax.shard_map(
        on_device, mesh=mesh, in_specs=in_specs, out_specs=out_specs, check_vma=False
    )
```

```python
import jax
import jax.numpy as jnp
from jax import lax
from jax.sharding import PartitionSpec as P


def from_behind(value, axis, steps):
    count = lax.axis_size(axis)
    pairs = [(source, (source + steps) % count) for source in range(count)]
    return lax.ppermute(value, axis, pairs)


def feat_permute(value, target):
    count = lax.axis_size("feat")
    return lax.ppermute(value, "feat", [(f, target(f)) for f in range(count)])


def gather_weight(weight):
    z_len = lax.axis_size("feat") // 4
    me = lax.axis_index("feat")
    own_core = me % 2
    own_z = (me // 2) % z_len
    own_xlo = me // (2 * z_len)
    xlo_stride = 2 * z_len
    partner = feat_permute(weight, lambda f: f ^ xlo_stride)
    pair = jnp.where(own_xlo == 0, jnp.stack([weight, partner]), jnp.stack([partner, weight]))
    got = [pair] + [
        feat_permute(pair, lambda f, k=k: (f // xlo_stride) * xlo_stride + ((f // 2 + k) % z_len) * 2 + f % 2)
        for k in range(1, z_len)
    ]
    return got


def assemble_weight(got, width):
    z_len = lax.axis_size("feat") // 4
    me = lax.axis_index("feat")
    own_core = me % 2
    own_z = (me // 2) % z_len
    order = (own_z - jnp.arange(z_len)) % z_len
    by_z = jnp.take(jnp.stack(got), order, axis=0)
    other = feat_permute(by_z, lambda f: f ^ 1)
    by_core = jnp.where(own_core == 0, jnp.stack([by_z, other]), jnp.stack([other, by_z]))
    return by_core.transpose(2, 1, 0, 3, 4).reshape(-1, width)


def on_device(node_features, adjacency, tile_row, tile_col, tile_count, weight, out_bias):
    feat_width = node_features.shape[0]
    rows_here = node_features.shape[1]
    tile_size = adjacency.shape[1]
    row_blocks = rows_here // tile_size
    cycle_len = lax.axis_size("row")
    slot_total = tile_row.shape[0] // cycle_len
    own_row = lax.axis_index("row")
    counts_here = tile_count[0]

    w_parts = gather_weight(weight)
    cols_out = lax.all_to_all(tile_col.reshape(cycle_len, slot_total), "row", 0, 0, tiled=True)
    blocks_t = node_features.reshape(feat_width, row_blocks, tile_size).transpose(1, 0, 2)

    tile_ids = jnp.arange(cycle_len * slot_total)
    live_all = (tile_ids % slot_total) < counts_here[tile_ids // slot_total]
    onehot_all = (
        (tile_row[:, None] == jnp.arange(row_blocks)[None, :]) & live_all[:, None]
    ).astype(jnp.float32).reshape(cycle_len, slot_total, row_blocks)

    def add_source(running, picked, source):
        tiles_part = lax.dynamic_slice_in_dim(adjacency, source * slot_total, slot_total, 0)
        onehot = lax.dynamic_index_in_dim(onehot_all, source, 0, keepdims=False)
        product = jnp.einsum("sfj,sji->fsi", picked, tiles_part, preferred_element_type=jnp.float32)
        return running + jnp.einsum("fsi,sr->fri", product, onehot)

    dests = (own_row + jnp.arange(1, cycle_len)) % cycle_len
    send_cols = jnp.take(cols_out, dests, axis=0).reshape(-1)
    picked_all = jnp.take(blocks_t, send_cols, axis=0).reshape(
        cycle_len - 1, slot_total, feat_width, tile_size
    )
    held = [from_behind(picked_all[k - 1], "row", k) for k in range(1, cycle_len)]
    own_cols = lax.dynamic_slice_in_dim(tile_col, own_row * slot_total, slot_total, 0)
    running = jnp.zeros((feat_width, row_blocks, tile_size), jnp.float32)
    running = add_source(running, jnp.take(blocks_t, own_cols, axis=0), own_row)
    for step_num in range(1, cycle_len):
        running = add_source(running, held[step_num - 1], (own_row - step_num) % cycle_len)
    w_parts, running = lax.optimization_barrier((tuple(w_parts), running))
    w_full = assemble_weight(list(w_parts), weight.shape[1])
    aggregated = running.reshape(feat_width, rows_here).astype(jnp.bfloat16)
    agg_t = lax.all_to_all(aggregated, "feat", 1, 0, tiled=True)
    pre_act = jnp.dot(w_full, agg_t, preferred_element_type=jnp.float32)
    act_t = jax.nn.relu(pre_act + out_bias[:, None]).astype(jnp.bfloat16)
    activated = lax.all_to_all(act_t, "feat", 0, 1, tiled=True)
    return activated


def solution(mesh):
    in_specs = (
        P("feat", "row"),
        P("row", None, None),
        P("row"),
        P("row"),
        P("row", None),
        P("feat", None),
        P(),
    )
    out_specs = P("feat", "row")
    return jax.shard_map(
        on_device, mesh=mesh, in_specs=in_specs, out_specs=out_specs, check_vma=False
    )
```

```python
import jax
import jax.numpy as jnp
from jax import lax
from jax.sharding import PartitionSpec as P


def from_behind(value, axis, steps):
    count = lax.axis_size(axis)
    pairs = [(source, (source + steps) % count) for source in range(count)]
    return lax.ppermute(value, axis, pairs)


def feat_permute(value, target):
    count = lax.axis_size("feat")
    return lax.ppermute(value, "feat", [(f, target(f)) for f in range(count)])


def swap_with(value, axis, mask):
    count = lax.axis_size(axis)
    return lax.ppermute(value, axis, [(i, i ^ mask) for i in range(count)])


def gather_weight(weight):
    z_len = lax.axis_size("feat") // 4
    pair = jnp.stack([weight, swap_with(weight, "feat", 2 * z_len)])
    return [pair] + [swap_with(pair, "feat", 2 * m) for m in range(1, z_len)]


def assemble_weight(got):
    by_m = jnp.stack(got)
    return jnp.stack([by_m, swap_with(by_m, "feat", 1)]).reshape(-1, by_m.shape[-1])


def arrival_order():
    z_len = lax.axis_size("feat") // 4
    me = lax.axis_index("feat")
    f = jnp.arange(lax.axis_size("feat"))
    c_rel = (f % 2) ^ (me % 2)
    m = ((f // 2) % z_len) ^ ((me // 2) % z_len)
    x_rel = (f // (2 * z_len)) ^ (me // (2 * z_len))
    return (c_rel * z_len + m) * 2 + x_rel


def on_device(node_features, adjacency, tile_row, tile_col, tile_count, weight, out_bias):
    feat_width = node_features.shape[0]
    rows_here = node_features.shape[1]
    tile_size = adjacency.shape[1]
    row_blocks = rows_here // tile_size
    cycle_len = lax.axis_size("row")
    slot_total = tile_row.shape[0] // cycle_len
    own_row = lax.axis_index("row")
    counts_here = tile_count[0]

    w_parts = gather_weight(weight)
    cols_out = lax.all_to_all(tile_col.reshape(cycle_len, slot_total), "row", 0, 0, tiled=True)
    blocks_t = node_features.reshape(feat_width, row_blocks, tile_size).transpose(1, 0, 2)

    tile_ids = jnp.arange(cycle_len * slot_total)
    live_all = (tile_ids % slot_total) < counts_here[tile_ids // slot_total]
    onehot_all = (
        (tile_row[:, None] == jnp.arange(row_blocks)[None, :]) & live_all[:, None]
    ).astype(jnp.float32).reshape(cycle_len, slot_total, row_blocks)

    def add_source(running, picked, source):
        tiles_part = lax.dynamic_slice_in_dim(adjacency, source * slot_total, slot_total, 0)
        onehot = lax.dynamic_index_in_dim(onehot_all, source, 0, keepdims=False)
        product = jnp.einsum("sfj,sji->fsi", picked, tiles_part, preferred_element_type=jnp.float32)
        return running + jnp.einsum("fsi,sr->fri", product, onehot)

    dests = jnp.bitwise_xor(own_row, jnp.arange(1, cycle_len))
    send_cols = jnp.take(cols_out, dests, axis=0).reshape(-1)
    picked_all = jnp.take(blocks_t, send_cols, axis=0).reshape(
        cycle_len - 1, slot_total, feat_width, tile_size
    )
    held = [swap_with(picked_all[m - 1], "row", m) for m in range(1, cycle_len)]
    own_cols = lax.dynamic_slice_in_dim(tile_col, own_row * slot_total, slot_total, 0)
    running = jnp.zeros((feat_width, row_blocks, tile_size), jnp.float32)
    running = add_source(running, jnp.take(blocks_t, own_cols, axis=0), own_row)
    for step_num in range(1, cycle_len):
        running = add_source(running, held[step_num - 1], jnp.bitwise_xor(own_row, step_num))
    w_parts, running = lax.optimization_barrier((tuple(w_parts), running))
    w_perm = assemble_weight(list(w_parts))
    aggregated = running.reshape(feat_width, rows_here).astype(jnp.bfloat16)
    agg_t = lax.all_to_all(aggregated, "feat", 1, 0, tiled=True)
    pre_perm = jnp.dot(w_perm, agg_t, preferred_element_type=jnp.float32)
    feat_count = lax.axis_size("feat")
    pre_act = jnp.take(
        pre_perm.reshape(feat_count, -1, pre_perm.shape[1]), arrival_order(), axis=0
    ).reshape(pre_perm.shape)
    act_t = jax.nn.relu(pre_act + out_bias[:, None]).astype(jnp.bfloat16)
    activated = lax.all_to_all(act_t, "feat", 0, 1, tiled=True)
    return activated


def solution(mesh):
    in_specs = (
        P("feat", "row"),
        P("row", None, None),
        P("row"),
        P("row"),
        P("row", None),
        P("feat", None),
        P(),
    )
    out_specs = P("feat", "row")
    return jax.shard_map(
        on_device, mesh=mesh, in_specs=in_specs, out_specs=out_specs, check_vma=False
    )
```

```python
import jax
import jax.numpy as jnp
from jax import lax
from jax.sharding import PartitionSpec as P


def swap_with(value, axis, mask):
    count = lax.axis_size(axis)
    return lax.ppermute(value, axis, [(i, i ^ mask) for i in range(count)])


def gather_weight(weight):
    z_len = lax.axis_size("feat") // 4
    pair = jnp.stack([weight, swap_with(weight, "feat", 2 * z_len)])
    return [pair] + [swap_with(pair, "feat", 2 * m) for m in range(1, z_len)]


def assemble_weight(got):
    by_m = jnp.stack(got)
    return jnp.stack([by_m, swap_with(by_m, "feat", 1)]).reshape(-1, by_m.shape[-1])


def arrival_order():
    z_len = lax.axis_size("feat") // 4
    me = lax.axis_index("feat")
    f = jnp.arange(lax.axis_size("feat"))
    c_rel = (f % 2) ^ (me % 2)
    m = ((f // 2) % z_len) ^ ((me // 2) % z_len)
    x_rel = (f // (2 * z_len)) ^ (me // (2 * z_len))
    return (c_rel * z_len + m) * 2 + x_rel


def on_device(node_features, adjacency, tile_row, tile_col, tile_count, weight, out_bias):
    feat_width = node_features.shape[0]
    rows_here = node_features.shape[1]
    tile_size = adjacency.shape[1]
    row_blocks = rows_here // tile_size
    cycle_len = lax.axis_size("row")
    slot_total = tile_row.shape[0] // cycle_len
    own_row = lax.axis_index("row")
    counts_here = tile_count[0]

    w_parts = gather_weight(weight)
    cols_out = lax.all_to_all(tile_col.reshape(cycle_len, slot_total), "row", 0, 0, tiled=True)
    blocks_t = node_features.reshape(feat_width, row_blocks, tile_size).transpose(1, 0, 2)

    tile_ids = jnp.arange(cycle_len * slot_total)
    live_all = (tile_ids % slot_total) < counts_here[tile_ids // slot_total]
    onehot_all = (
        (tile_row[:, None] == jnp.arange(row_blocks)[None, :]) & live_all[:, None]
    ).astype(jnp.float32).reshape(cycle_len, slot_total, row_blocks)

    def add_source(running, picked, source):
        tiles_part = lax.dynamic_slice_in_dim(adjacency, source * slot_total, slot_total, 0)
        onehot = lax.dynamic_index_in_dim(onehot_all, source, 0, keepdims=False)
        product = jnp.einsum("sfj,sji->fsi", picked, tiles_part, preferred_element_type=jnp.float32)
        return running + jnp.einsum("fsi,sr->fri", product, onehot)

    dests = jnp.bitwise_xor(own_row, jnp.arange(1, cycle_len))
    send_cols = jnp.take(cols_out, dests, axis=0).reshape(-1)
    picked_all = jnp.take(blocks_t, send_cols, axis=0).reshape(
        cycle_len - 1, slot_total, feat_width, tile_size
    )
    held = [swap_with(picked_all[m - 1], "row", m) for m in range(1, cycle_len)]
    own_cols = lax.dynamic_slice_in_dim(tile_col, own_row * slot_total, slot_total, 0)
    running = jnp.zeros((feat_width, row_blocks, tile_size), jnp.float32)
    running = add_source(running, jnp.take(blocks_t, own_cols, axis=0), own_row)
    for step_num in range(1, cycle_len):
        running = add_source(running, held[step_num - 1], jnp.bitwise_xor(own_row, step_num))
    w_perm = assemble_weight(w_parts)
    aggregated = running.reshape(feat_width, rows_here).astype(jnp.bfloat16)
    agg_t = lax.all_to_all(aggregated, "feat", 1, 0, tiled=True)
    pre_perm = jnp.dot(w_perm, agg_t, preferred_element_type=jnp.float32)
    feat_count = lax.axis_size("feat")
    order = arrival_order()
    inverse = jnp.zeros_like(order).at[order].set(jnp.arange(feat_count))
    bias_perm = jnp.take(out_bias.reshape(feat_count, -1), inverse, axis=0).reshape(-1)
    act_perm = jax.nn.relu(pre_perm + bias_perm[:, None]).astype(jnp.bfloat16)
    act_t = jnp.take(
        act_perm.reshape(feat_count, -1, act_perm.shape[1]), order, axis=0
    ).reshape(act_perm.shape)
    activated = lax.all_to_all(act_t, "feat", 0, 1, tiled=True)
    return activated


def solution(mesh):
    in_specs = (
        P("feat", "row"),
        P("row", None, None),
        P("row"),
        P("row"),
        P("row", None),
        P("feat", None),
        P(),
    )
    out_specs = P("feat", "row")

    return jax.shard_map(on_device, mesh=mesh, in_specs=in_specs, out_specs=out_specs, check_vma=False)
```

```python
import jax
import jax.numpy as jnp
from jax import lax
from jax.sharding import PartitionSpec as P


def swap_with(value, axis, mask):
    count = lax.axis_size(axis)
    return lax.ppermute(value, axis, [(i, i ^ mask) for i in range(count)])


def weight_bits():
    bits = lax.axis_size("feat").bit_length() - 1
    return [bits - 1] + list(range(bits - 2, 0, -1)) + [0]


def gather_weight(held, bits):
    me = lax.axis_index("feat")
    for bit in bits:
        theirs = swap_with(held, "feat", 1 << bit)
        mine_low = ((me >> bit) & 1) == 0
        low = jnp.where(mine_low, held, theirs)
        high = jnp.where(mine_low, theirs, held)
        held = jnp.stack([low, high], axis=1).reshape(-1, *held.shape[1:])
    return held


def on_device(node_features, adjacency, tile_row, tile_col, tile_count, weight, out_bias):
    feat_width = node_features.shape[0]
    rows_here = node_features.shape[1]
    tile_size = adjacency.shape[1]
    row_blocks = rows_here // tile_size
    cycle_len = lax.axis_size("row")
    slot_total = tile_row.shape[0] // cycle_len
    own_row = lax.axis_index("row")
    counts_here = tile_count[0]

    bits = weight_bits()
    w_mid = gather_weight(weight.reshape(1, *weight.shape), bits[:3])
    cols_out = lax.all_to_all(tile_col.reshape(cycle_len, slot_total), "row", 0, 0, tiled=True)
    w_mid, cols_out = lax.optimization_barrier((w_mid, cols_out))
    blocks_t = node_features.reshape(feat_width, row_blocks, tile_size).transpose(1, 0, 2)

    tile_ids = jnp.arange(cycle_len * slot_total)
    live_all = (tile_ids % slot_total) < counts_here[tile_ids // slot_total]
    onehot_all = (
        (tile_row[:, None] == jnp.arange(row_blocks)[None, :]) & live_all[:, None]
    ).astype(jnp.float32).reshape(cycle_len, slot_total, row_blocks)

    def add_source(running, picked, source):
        tiles_part = lax.dynamic_slice_in_dim(adjacency, source * slot_total, slot_total, 0)
        onehot = lax.dynamic_index_in_dim(onehot_all, source, 0, keepdims=False)
        product = jnp.einsum("sfj,sji->fsi", picked, tiles_part, preferred_element_type=jnp.float32)
        return running + jnp.einsum("fsi,sr->fri", product, onehot)

    dests = jnp.bitwise_xor(own_row, jnp.arange(1, cycle_len))
    send_cols = jnp.take(cols_out, dests, axis=0).reshape(-1)
    picked_all = jnp.take(blocks_t, send_cols, axis=0).reshape(
        cycle_len - 1, slot_total, feat_width, tile_size
    )
    held = [swap_with(picked_all[m - 1], "row", m) for m in range(1, cycle_len)]
    own_cols = lax.dynamic_slice_in_dim(tile_col, own_row * slot_total, slot_total, 0)
    running = jnp.zeros((feat_width, row_blocks, tile_size), jnp.float32)
    running = add_source(running, jnp.take(blocks_t, own_cols, axis=0), own_row)
    for step_num in range(1, cycle_len):
        running = add_source(running, held[step_num - 1], jnp.bitwise_xor(own_row, step_num))
    w_mid, _ = lax.optimization_barrier((gather_weight(w_mid, bits[3:4]), running))
    w_full = gather_weight(w_mid, bits[4:]).reshape(-1, weight.shape[1])
    aggregated = running.reshape(feat_width, rows_here).astype(jnp.bfloat16)
    agg_t = lax.all_to_all(aggregated, "feat", 1, 0, tiled=True)
    pre_act = jnp.dot(w_full, agg_t, preferred_element_type=jnp.float32)
    act_t = jax.nn.relu(pre_act + out_bias[:, None]).astype(jnp.bfloat16)
    activated = lax.all_to_all(act_t, "feat", 0, 1, tiled=True)
    return activated


def solution(mesh):
    in_specs = (
        P("feat", "row"),
        P("row", None, None),
        P("row"),
        P("row"),
        P("row", None),
        P("feat", None),
        P(),
    )
    out_specs = P("feat", "row")

    return jax.shard_map(on_device, mesh=mesh, in_specs=in_specs, out_specs=out_specs, check_vma=False)
```

```python
import jax
import jax.numpy as jnp
from jax import lax
from jax.sharding import PartitionSpec as P


def swap_with(value, axis, mask):
    count = lax.axis_size(axis)
    return lax.ppermute(value, axis, [(i, i ^ mask) for i in range(count)])


def gather_weight(weight):
    feat_count = lax.axis_size("feat")
    me = lax.axis_index("feat")
    bits = feat_count.bit_length() - 1
    order = [bits - 1] + list(range(bits - 2, 0, -1)) + [0]
    held = weight.reshape(1, -1, weight.shape[1])
    for bit in order:
        theirs = swap_with(held, "feat", 1 << bit)
        mine_low = ((me >> bit) & 1) == 0
        low = jnp.where(mine_low, held, theirs)
        high = jnp.where(mine_low, theirs, held)
        held = jnp.stack([low, high], axis=1).reshape(-1, *held.shape[1:])
    return held.reshape(-1, weight.shape[1])


def on_device(node_features, adjacency, tile_row, tile_col, tile_count, weight, out_bias):
    feat_width = node_features.shape[0]
    rows_here = node_features.shape[1]
    tile_size = adjacency.shape[1]
    row_blocks = rows_here // tile_size
    cycle_len = lax.axis_size("row")
    slot_total = tile_row.shape[0] // cycle_len
    own_row = lax.axis_index("row")
    counts_here = tile_count[0]

    w_full = gather_weight(weight)
    cols_out = lax.all_to_all(tile_col.reshape(cycle_len, slot_total), "row", 0, 0, tiled=True)
    blocks_t = node_features.reshape(feat_width, row_blocks, tile_size).transpose(1, 0, 2)

    tile_ids = jnp.arange(cycle_len * slot_total)
    live_all = (tile_ids % slot_total) < counts_here[tile_ids // slot_total]
    onehot_all = (
        (tile_row[:, None] == jnp.arange(row_blocks)[None, :]) & live_all[:, None]
    ).astype(jnp.float32).reshape(cycle_len, slot_total, row_blocks)

    def add_source(running, picked, source):
        tiles_part = lax.dynamic_slice_in_dim(adjacency, source * slot_total, slot_total, 0)
        onehot = lax.dynamic_index_in_dim(onehot_all, source, 0, keepdims=False)
        product = jnp.einsum("sfj,sji->fsi", picked, tiles_part, preferred_element_type=jnp.float32)
        return running + jnp.einsum("fsi,sr->fri", product, onehot)

    whole = (1, 3)
    picked_m = [m for m in range(1, cycle_len) if m not in whole]
    dests = jnp.bitwise_xor(own_row, jnp.array(picked_m))
    send_cols = jnp.take(cols_out, dests, axis=0).reshape(-1)
    picked_all = jnp.take(blocks_t, send_cols, axis=0).reshape(
        len(picked_m), slot_total, feat_width, tile_size
    )

    def own_cols_of(source):
        return lax.dynamic_slice_in_dim(tile_col, source * slot_total, slot_total, 0)

    held = {}
    for m in whole:
        block = swap_with(node_features, "row", m)
        block_t = block.reshape(feat_width, row_blocks, tile_size).transpose(1, 0, 2)
        held[m] = jnp.take(block_t, own_cols_of(jnp.bitwise_xor(own_row, m)), axis=0)
    for i, m in enumerate(picked_m):
        held[m] = swap_with(picked_all[i], "row", m)
    running = jnp.zeros((feat_width, row_blocks, tile_size), jnp.float32)
    running = add_source(running, jnp.take(blocks_t, own_cols_of(own_row), axis=0), own_row)
    for step_num in range(1, cycle_len):
        running = add_source(running, held[step_num], jnp.bitwise_xor(own_row, step_num))
    aggregated = running.reshape(feat_width, rows_here).astype(jnp.bfloat16)
    agg_t = lax.all_to_all(aggregated, "feat", 1, 0, tiled=True)
    pre_act = jnp.dot(w_full, agg_t, preferred_element_type=jnp.float32)
    act_t = jax.nn.relu(pre_act + out_bias[:, None]).astype(jnp.bfloat16)
    activated = lax.all_to_all(act_t, "feat", 0, 1, tiled=True)
    return activated


def solution(mesh):
    in_specs = (
        P("feat", "row"),
        P("row", None, None),
        P("row"),
        P("row"),
        P("row", None),
        P("feat", None),
        P(),
    )
    out_specs = P("feat", "row")

    return jax.shard_map(on_device, mesh=mesh, in_specs=in_specs, out_specs=out_specs, check_vma=False)
```

```python
import jax
import jax.numpy as jnp
from jax import lax
from jax.sharding import PartitionSpec as P


def swap_with(value, axis, mask):
    count = lax.axis_size(axis)
    return lax.ppermute(value, axis, [(i, i ^ mask) for i in range(count)])


def gather_weight(weight):
    feat_count = lax.axis_size("feat")
    me = lax.axis_index("feat")
    bits = feat_count.bit_length() - 1
    order = [bits - 1] + list(range(bits - 2, 0, -1)) + [0]
    held = weight.reshape(1, -1, weight.shape[1])
    for bit in order:
        theirs = swap_with(held, "feat", 1 << bit)
        mine_low = ((me >> bit) & 1) == 0
        low = jnp.where(mine_low, held, theirs)
        high = jnp.where(mine_low, theirs, held)
        held = jnp.stack([low, high], axis=1).reshape(-1, *held.shape[1:])
    return held.reshape(-1, weight.shape[1])


def on_device(node_features, adjacency, tile_row, tile_col, tile_count, weight, out_bias):
    feat_width = node_features.shape[0]
    rows_here = node_features.shape[1]
    tile_size = adjacency.shape[1]
    row_blocks = rows_here // tile_size
    cycle_len = lax.axis_size("row")
    slot_total = tile_row.shape[0] // cycle_len
    own_row = lax.axis_index("row")
    counts_here = tile_count[0]

    w_full = gather_weight(weight)
    cols_out = lax.all_to_all(tile_col.reshape(cycle_len, slot_total), "row", 0, 0, tiled=True)
    blocks_t = node_features.reshape(feat_width, row_blocks, tile_size).transpose(1, 0, 2)

    tile_ids = jnp.arange(cycle_len * slot_total)
    live_all = (tile_ids % slot_total) < counts_here[tile_ids // slot_total]
    onehot_all = (
        (tile_row[:, None] == jnp.arange(row_blocks)[None, :]) & live_all[:, None]
    ).astype(jnp.float32).reshape(cycle_len, slot_total, row_blocks)

    def add_source(running, picked, source):
        tiles_part = lax.dynamic_slice_in_dim(adjacency, source * slot_total, slot_total, 0)
        onehot = lax.dynamic_index_in_dim(onehot_all, source, 0, keepdims=False)
        product = jnp.einsum("sfj,sji->fsi", picked, tiles_part, preferred_element_type=jnp.float32)
        return running + jnp.einsum("fsi,sr->fri", product, onehot)

    dests = jnp.bitwise_xor(own_row, jnp.arange(1, cycle_len))
    send_cols = jnp.take(cols_out, dests, axis=0).reshape(-1)
    picked_all = jnp.take(blocks_t, send_cols, axis=0).reshape(
        cycle_len - 1, slot_total, feat_width, tile_size
    )
    held = [swap_with(picked_all[m - 1], "row", m) for m in range(1, cycle_len)]
    own_cols = lax.dynamic_slice_in_dim(tile_col, own_row * slot_total, slot_total, 0)
    running = jnp.zeros((feat_width, row_blocks, tile_size), jnp.float32)
    running = add_source(running, jnp.take(blocks_t, own_cols, axis=0), own_row)
    for step_num in range(1, cycle_len):
        running = add_source(running, held[step_num - 1], jnp.bitwise_xor(own_row, step_num))
    aggregated = running.reshape(feat_width, rows_here).astype(jnp.bfloat16)
    agg_t = lax.all_to_all(aggregated, "feat", 1, 0, tiled=True)
    pre_act = jnp.dot(w_full, agg_t, preferred_element_type=jnp.float32)
    act_t = jax.nn.relu(pre_act + out_bias[:, None]).astype(jnp.bfloat16)
    activated = lax.all_to_all(act_t, "feat", 0, 1, tiled=True)
    return activated


def solution(mesh):
    in_specs = (
        P("feat", "row"),
        P("row", None, None),
        P("row"),
        P("row"),
        P("row", None),
        P("feat", None),
        P(),
    )
    out_specs = P("feat", "row")

    return jax.shard_map(on_device, mesh=mesh, in_specs=in_specs, out_specs=out_specs, check_vma=False)
```

```python
import jax
import jax.numpy as jnp
from jax import lax
from jax.sharding import PartitionSpec as P


def swap_with(value, axis, mask):
    count = lax.axis_size(axis)
    return lax.ppermute(value, axis, [(i, i ^ mask) for i in range(count)])


def weight_bits():
    bits = lax.axis_size("feat").bit_length() - 1
    return [bits - 1] + list(range(bits - 2, 0, -1)) + [0]


def gather_weight(held, bits):
    me = lax.axis_index("feat")
    for bit in bits:
        theirs = swap_with(held, "feat", 1 << bit)
        mine_low = ((me >> bit) & 1) == 0
        low = jnp.where(mine_low, held, theirs)
        high = jnp.where(mine_low, theirs, held)
        held = jnp.stack([low, high], axis=1).reshape(-1, *held.shape[1:])
    return held


def on_device(node_features, adjacency, tile_row, tile_col, tile_count, weight, out_bias):
    feat_width = node_features.shape[0]
    rows_here = node_features.shape[1]
    tile_size = adjacency.shape[1]
    row_blocks = rows_here // tile_size
    cycle_len = lax.axis_size("row")
    slot_total = tile_row.shape[0] // cycle_len
    own_row = lax.axis_index("row")
    counts_here = tile_count[0]

    bits = weight_bits()
    w_mid = gather_weight(weight.reshape(1, *weight.shape), bits[:2])
    cols_out = lax.all_to_all(tile_col.reshape(cycle_len, slot_total), "row", 0, 0, tiled=True)
    w_mid, cols_out = lax.optimization_barrier((w_mid, cols_out))
    w_full = gather_weight(w_mid, bits[2:]).reshape(-1, weight.shape[1])
    blocks_t = node_features.reshape(feat_width, row_blocks, tile_size).transpose(1, 0, 2)

    tile_ids = jnp.arange(cycle_len * slot_total)
    live_all = (tile_ids % slot_total) < counts_here[tile_ids // slot_total]
    onehot_all = (
        (tile_row[:, None] == jnp.arange(row_blocks)[None, :]) & live_all[:, None]
    ).astype(jnp.float32).reshape(cycle_len, slot_total, row_blocks)

    def add_source(running, picked, source):
        tiles_part = lax.dynamic_slice_in_dim(adjacency, source * slot_total, slot_total, 0)
        onehot = lax.dynamic_index_in_dim(onehot_all, source, 0, keepdims=False)
        product = jnp.einsum("sfj,sji->fsi", picked, tiles_part, preferred_element_type=jnp.float32)
        return running + jnp.einsum("fsi,sr->fri", product, onehot)

    dests = jnp.bitwise_xor(own_row, jnp.arange(1, cycle_len))
    send_cols = jnp.take(cols_out, dests, axis=0).reshape(-1)
    picked_all = jnp.take(blocks_t, send_cols, axis=0).reshape(
        cycle_len - 1, slot_total, feat_width, tile_size
    )
    held = [swap_with(picked_all[m - 1], "row", m) for m in range(1, cycle_len)]
    own_cols = lax.dynamic_slice_in_dim(tile_col, own_row * slot_total, slot_total, 0)
    running = jnp.zeros((feat_width, row_blocks, tile_size), jnp.float32)
    running = add_source(running, jnp.take(blocks_t, own_cols, axis=0), own_row)
    for step_num in range(1, cycle_len):
        running = add_source(running, held[step_num - 1], jnp.bitwise_xor(own_row, step_num))
    aggregated = running.reshape(feat_width, rows_here).astype(jnp.bfloat16)
    agg_t = lax.all_to_all(aggregated, "feat", 1, 0, tiled=True)
    pre_act = jnp.dot(w_full, agg_t, preferred_element_type=jnp.float32)
    act_t = jax.nn.relu(pre_act + out_bias[:, None]).astype(jnp.bfloat16)
    activated = lax.all_to_all(act_t, "feat", 0, 1, tiled=True)
    return activated


def solution(mesh):
    in_specs = (
        P("feat", "row"),
        P("row", None, None),
        P("row"),
        P("row"),
        P("row", None),
        P("feat", None),
        P(),
    )
    out_specs = P("feat", "row")

    return jax.shard_map(on_device, mesh=mesh, in_specs=in_specs, out_specs=out_specs, check_vma=False)
```

```python
import jax
import jax.numpy as jnp
from jax import lax
from jax.sharding import PartitionSpec as P


def swap_with(value, axis, mask):
    count = lax.axis_size(axis)
    return lax.ppermute(value, axis, [(i, i ^ mask) for i in range(count)])


def gather_weight(weight):
    feat_count = lax.axis_size("feat")
    me = lax.axis_index("feat")
    bits = feat_count.bit_length() - 1
    order = [bits - 1] + list(range(bits - 2, 0, -1)) + [0]
    held = weight.reshape(1, -1, weight.shape[1])
    for bit in order:
        theirs = swap_with(held, "feat", 1 << bit)
        mine_low = ((me >> bit) & 1) == 0
        low = jnp.where(mine_low, held, theirs)
        high = jnp.where(mine_low, theirs, held)
        held = jnp.stack([low, high], axis=1).reshape(-1, *held.shape[1:])
    return held.reshape(-1, weight.shape[1])


def on_device(node_features, adjacency, tile_row, tile_col, tile_count, weight, out_bias):
    feat_width = node_features.shape[0]
    rows_here = node_features.shape[1]
    tile_size = adjacency.shape[1]
    row_blocks = rows_here // tile_size
    cycle_len = lax.axis_size("row")
    slot_total = tile_row.shape[0] // cycle_len
    own_row = lax.axis_index("row")
    counts_here = tile_count[0]

    w_full = gather_weight(weight)
    cols_out = lax.all_to_all(tile_col.reshape(cycle_len, slot_total), "row", 0, 0, tiled=True)
    blocks_t = node_features.reshape(feat_width, row_blocks, tile_size).transpose(1, 0, 2)

    tile_ids = jnp.arange(cycle_len * slot_total)
    live_all = (tile_ids % slot_total) < counts_here[tile_ids // slot_total]
    onehot_all = (
        (tile_row[:, None] == jnp.arange(row_blocks)[None, :]) & live_all[:, None]
    ).astype(jnp.float32).reshape(cycle_len, slot_total, row_blocks)

    def add_source(running, picked, source):
        tiles_part = lax.dynamic_slice_in_dim(adjacency, source * slot_total, slot_total, 0)
        onehot = lax.dynamic_index_in_dim(onehot_all, source, 0, keepdims=False)
        product = jnp.einsum("sfj,sji->fsi", picked, tiles_part, preferred_element_type=jnp.float32)
        return running + jnp.einsum("fsi,sr->fri", product, onehot)

    dests = jnp.bitwise_xor(own_row, jnp.arange(1, cycle_len))
    send_cols = jnp.take(cols_out, dests, axis=0).reshape(-1)
    picked_all = jnp.take(blocks_t, send_cols, axis=0).reshape(
        cycle_len - 1, slot_total, feat_width, tile_size
    )
    held = {}
    for m in range(1, cycle_len):
        held[m] = swap_with(picked_all[m - 1], "row", m)
    own_cols = lax.dynamic_slice_in_dim(tile_col, own_row * slot_total, slot_total, 0)
    running = jnp.zeros((feat_width, row_blocks, tile_size), jnp.float32)
    running = add_source(running, jnp.take(blocks_t, own_cols, axis=0), own_row)
    for step_num in range(1, cycle_len):
        running = add_source(running, held[step_num], jnp.bitwise_xor(own_row, step_num))
    aggregated = running.reshape(feat_width, rows_here).astype(jnp.bfloat16)
    agg_t = lax.all_to_all(aggregated, "feat", 1, 0, tiled=True)
    pre_act = jnp.dot(w_full, agg_t, preferred_element_type=jnp.float32)
    act_t = jax.nn.relu(pre_act + out_bias[:, None]).astype(jnp.bfloat16)
    activated = lax.all_to_all(act_t, "feat", 0, 1, tiled=True)
    return activated


def solution(mesh):
    in_specs = (
        P("feat", "row"),
        P("row", None, None),
        P("row"),
        P("row"),
        P("row", None),
        P("feat", None),
        P(),
    )
    out_specs = P("feat", "row")

    return jax.shard_map(on_device, mesh=mesh, in_specs=in_specs, out_specs=out_specs, check_vma=False)
```

```python
import jax
import jax.numpy as jnp
from jax import lax
from jax.sharding import PartitionSpec as P


def swap_with(value, axis, mask):
    count = lax.axis_size(axis)
    return lax.ppermute(value, axis, [(i, i ^ mask) for i in range(count)])


def weight_bits():
    bits = lax.axis_size("feat").bit_length() - 1
    return [bits - 1] + list(range(bits - 2, 0, -1)) + [0]


def gather_weight(held, bits):
    me = lax.axis_index("feat")
    for bit in bits:
        theirs = swap_with(held, "feat", 1 << bit)
        mine_low = ((me >> bit) & 1) == 0
        low = jnp.where(mine_low, held, theirs)
        high = jnp.where(mine_low, theirs, held)
        held = jnp.stack([low, high], axis=1).reshape(-1, *held.shape[1:])
    return held


def on_device(node_features, adjacency, tile_row, tile_col, tile_count, weight, out_bias):
    feat_width = node_features.shape[0]
    rows_here = node_features.shape[1]
    tile_size = adjacency.shape[1]
    row_blocks = rows_here // tile_size
    cycle_len = lax.axis_size("row")
    slot_total = tile_row.shape[0] // cycle_len
    own_row = lax.axis_index("row")
    counts_here = tile_count[0]

    bits = weight_bits()
    w_mid = gather_weight(weight.reshape(1, *weight.shape), bits[:-1])
    cols_out = lax.all_to_all(tile_col.reshape(cycle_len, slot_total), "row", 0, 0, tiled=True)
    blocks_t = node_features.reshape(feat_width, row_blocks, tile_size).transpose(1, 0, 2)

    tile_ids = jnp.arange(cycle_len * slot_total)
    live_all = (tile_ids % slot_total) < counts_here[tile_ids // slot_total]
    onehot_all = (
        (tile_row[:, None] == jnp.arange(row_blocks)[None, :]) & live_all[:, None]
    ).astype(jnp.float32).reshape(cycle_len, slot_total, row_blocks)

    def add_source(running, picked, source):
        tiles_part = lax.dynamic_slice_in_dim(adjacency, source * slot_total, slot_total, 0)
        onehot = lax.dynamic_index_in_dim(onehot_all, source, 0, keepdims=False)
        product = jnp.einsum("sfj,sji->fsi", picked, tiles_part, preferred_element_type=jnp.float32)
        return running + jnp.einsum("fsi,sr->fri", product, onehot)

    dests = jnp.bitwise_xor(own_row, jnp.arange(1, cycle_len))
    send_cols = jnp.take(cols_out, dests, axis=0).reshape(-1)
    picked_all = jnp.take(blocks_t, send_cols, axis=0).reshape(
        cycle_len - 1, slot_total, feat_width, tile_size
    )
    held = [swap_with(picked_all[m - 1], "row", m) for m in range(1, cycle_len)]
    own_cols = lax.dynamic_slice_in_dim(tile_col, own_row * slot_total, slot_total, 0)
    running = jnp.zeros((feat_width, row_blocks, tile_size), jnp.float32)
    running = add_source(running, jnp.take(blocks_t, own_cols, axis=0), own_row)
    for step_num in range(1, cycle_len):
        running = add_source(running, held[step_num - 1], jnp.bitwise_xor(own_row, step_num))
    w_mid, _ = lax.optimization_barrier((w_mid, running))
    w_full = gather_weight(w_mid, bits[-1:]).reshape(-1, weight.shape[1])
    aggregated = running.reshape(feat_width, rows_here).astype(jnp.bfloat16)
    agg_t = lax.all_to_all(aggregated, "feat", 1, 0, tiled=True)
    pre_act = jnp.dot(w_full, agg_t, preferred_element_type=jnp.float32)
    act_t = jax.nn.relu(pre_act + out_bias[:, None]).astype(jnp.bfloat16)
    activated = lax.all_to_all(act_t, "feat", 0, 1, tiled=True)
    return activated


def solution(mesh):
    in_specs = (
        P("feat", "row"),
        P("row", None, None),
        P("row"),
        P("row"),
        P("row", None),
        P("feat", None),
        P(),
    )
    out_specs = P("feat", "row")

    return jax.shard_map(on_device, mesh=mesh, in_specs=in_specs, out_specs=out_specs, check_vma=False)
```

```python
import jax
import jax.numpy as jnp
from jax import lax
from jax.sharding import PartitionSpec as P


def swap_with(value, axis, mask):
    count = lax.axis_size(axis)
    return lax.ppermute(value, axis, [(i, i ^ mask) for i in range(count)])


def gather_weight(weight):
    feat_count = lax.axis_size("feat")
    me = lax.axis_index("feat")
    bits = feat_count.bit_length() - 1
    order = list(range(bits - 2, 0, -1)) + [bits - 1, 0]
    held = weight.reshape(1, -1, weight.shape[1])
    done = []
    for bit in order:
        theirs = swap_with(held, "feat", 1 << bit)
        mine_low = ((me >> bit) & 1) == 0
        low = jnp.where(mine_low, held, theirs)
        high = jnp.where(mine_low, theirs, held)
        above = 2 ** sum(1 for b in done if b > bit)
        pair = jnp.stack(
            [low.reshape(above, -1, *held.shape[1:]), high.reshape(above, -1, *held.shape[1:])], axis=1
        )
        held = pair.reshape(-1, *held.shape[1:])
        done.append(bit)
    return held.reshape(-1, weight.shape[1])


def on_device(node_features, adjacency, tile_row, tile_col, tile_count, weight, out_bias):
    feat_width = node_features.shape[0]
    rows_here = node_features.shape[1]
    tile_size = adjacency.shape[1]
    row_blocks = rows_here // tile_size
    cycle_len = lax.axis_size("row")
    slot_total = tile_row.shape[0] // cycle_len
    own_row = lax.axis_index("row")
    counts_here = tile_count[0]

    w_full = gather_weight(weight)
    cols_out = lax.all_to_all(tile_col.reshape(cycle_len, slot_total), "row", 0, 0, tiled=True)
    blocks_t = node_features.reshape(feat_width, row_blocks, tile_size).transpose(1, 0, 2)

    tile_ids = jnp.arange(cycle_len * slot_total)
    live_all = (tile_ids % slot_total) < counts_here[tile_ids // slot_total]
    onehot_all = (
        (tile_row[:, None] == jnp.arange(row_blocks)[None, :]) & live_all[:, None]
    ).astype(jnp.float32).reshape(cycle_len, slot_total, row_blocks)

    def add_source(running, picked, source):
        tiles_part = lax.dynamic_slice_in_dim(adjacency, source * slot_total, slot_total, 0)
        onehot = lax.dynamic_index_in_dim(onehot_all, source, 0, keepdims=False)
        product = jnp.einsum("sfj,sji->fsi", picked, tiles_part, preferred_element_type=jnp.float32)
        return running + jnp.einsum("fsi,sr->fri", product, onehot)

    dests = jnp.bitwise_xor(own_row, jnp.arange(1, cycle_len))
    send_cols = jnp.take(cols_out, dests, axis=0).reshape(-1)
    picked_all = jnp.take(blocks_t, send_cols, axis=0).reshape(
        cycle_len - 1, slot_total, feat_width, tile_size
    )
    held = [swap_with(picked_all[m - 1], "row", m) for m in range(1, cycle_len)]
    own_cols = lax.dynamic_slice_in_dim(tile_col, own_row * slot_total, slot_total, 0)
    running = jnp.zeros((feat_width, row_blocks, tile_size), jnp.float32)
    running = add_source(running, jnp.take(blocks_t, own_cols, axis=0), own_row)
    for step_num in range(1, cycle_len):
        running = add_source(running, held[step_num - 1], jnp.bitwise_xor(own_row, step_num))
    aggregated = running.reshape(feat_width, rows_here).astype(jnp.bfloat16)
    agg_t = lax.all_to_all(aggregated, "feat", 1, 0, tiled=True)
    pre_act = jnp.dot(w_full, agg_t, preferred_element_type=jnp.float32)
    act_t = jax.nn.relu(pre_act + out_bias[:, None]).astype(jnp.bfloat16)
    activated = lax.all_to_all(act_t, "feat", 0, 1, tiled=True)
    return activated


def solution(mesh):
    in_specs = (
        P("feat", "row"),
        P("row", None, None),
        P("row"),
        P("row"),
        P("row", None),
        P("feat", None),
        P(),
    )
    out_specs = P("feat", "row")

    return jax.shard_map(on_device, mesh=mesh, in_specs=in_specs, out_specs=out_specs, check_vma=False)
```
